512 devices in a mesh: dp: 16 (over y, core), tensor: 32 (over z, x).
Axes of the slice: x: 4, y: 8, z: 8, core: 2. Of those that a mesh axis runs over, the one named last changes fastest.
Arguments:
- layer_input: bfloat16 [65536, 8192], P('dp', 'tensor'), may hold values from -6 to 6
- output_grad: bfloat16 [65536, 1024], P(('dp', 'tensor')), may hold values from -6 to 6
- key_weight: bfloat16 [8192, 1024], P('tensor'), may hold values from -0.0625 to 0.0625
- adapter_down: bfloat16 [128, 16, 8192], P('dp', None, 'tensor'), may hold values from -0.0625 to 0.0625
- adapter_up: bfloat16 [128, 16, 1024], P('dp', None, 'tensor'), may hold values from -0.1875 to 0.1875
- segment_adapter: int32 [512], replicated, may hold values from 0 to 127
- adapter_slot: int32 [128], replicated, may hold values from 0 to 127, each once
- live_segments: int32 [16], P('dp'), may hold values from 1 to 32, as said below
Outputs:
- input_grad: bfloat16 [65536, 8192], P('dp', 'tensor')
- down_grad: bfloat16 [128, 16, 8192], P('dp', None, 'tensor')
- up_grad: bfloat16 [128, 16, 1024], P('dp', None, 'tensor')
The draws below stay inside these ranges and needn't reach their ends.
Inputs may be any that keep to these rules, and one draw needn't show every extreme that they name: `live_segments`: some data group has all 32 segments live; a group's segments at or past its count are padding.
All inputs are finite; a program needn't handle non-finite values.
Results may differ from the reference program's by a relative error of at most 0.0057.
Values may be sent and summed in bfloat16 or wider, within the bound.
No kernel may reach another device: no remote copies, remote signals or barrier semaphores. Data moves between devices by JAX's collectives and lax.ppermute only.
A program may use at most 64 MiB of HBM per device.

```python
import math
import jax
import jax.numpy as jnp
import numpy as np
from jax import lax

D = 8192
KW = 1024
R = 16
ADAPTERS = 128
SEG = 128
TOK_GROUP = 4096
TOKENS = 65536
SEGS_GROUP = 32
SEGS = 512
N_DP = 16


def draw_live_segments(key, part):
    base = jax.random.fold_in(key, 11)
    first_key, second_key = jax.random.split(base)
    counts = jax.random.randint(first_key, (N_DP,), 1, SEGS_GROUP + 1)
    full_group = jax.random.randint(second_key, (), 0, N_DP)
    filled = jnp.where(jnp.arange(N_DP) == full_group, SEGS_GROUP, counts)
    return filled.astype(jnp.int32)


def place_ends(values, own_key, low, largest):
    dims = values.shape
    spot = [jax.random.randint(jax.random.fold_in(own_key, axis), (), 0, dims[axis]) for axis in range(len(dims))]
    values = values.at[tuple(spot)].set(low)
    longest = dims.index(max(dims))
    spot[longest] = (spot[longest] + 1) % dims[longest]
    return values.at[tuple(spot)].set(largest)


def block_scale(own_key, extent, pieces, least, top_value):
    level = 1.0
    for position, parts in pieces:
        draws = jax.random.uniform(jax.random.fold_in(jax.random.fold_in(own_key, 6), position), (parts,), jnp.float32, least / len(pieces), top_value / len(pieces))
        level = level * jnp.repeat(jnp.exp(draws), extent[position] // parts).reshape((-1,) + (1,) * (len(extent) - 1 - position))
    return level


def rank_table(count, lean):
    weights = [(1 << 20) // math.isqrt(standing ** lean) + 1 for standing in range(1, count + 1)]
    width = 1 + sum(weights) // (1 << 30)
    return np.cumsum(np.array([max(1, weight // width) for weight in weights]))


def skewed_ids(key, shape, number_of, slope):
    table = rank_table(number_of, slope)
    pick = jax.random.randint(jax.random.fold_in(key, 1), shape, 0, int(table[number_of - 1]))
    grade = jnp.searchsorted(jnp.asarray(table, jnp.int32), pick, side="right")
    return jax.random.permutation(jax.random.fold_in(key, 2), number_of)[grade].astype(jnp.int32)


def noise(stream_key, extent, scale, limit, cuts=(), kind=jnp.bfloat16):
    values = scale * jax.random.normal(stream_key, extent, jnp.float32)
    if cuts:
        values = values * block_scale(stream_key, extent, cuts, -0.22, 0.18)
    return jnp.clip(values, -limit, limit).astype(kind)


def setup_inputs(seed: int = 0) -> dict:
    streams_of = jax.random.split(jax.random.key(seed), 9)
    return {
        "layer_input": noise(streams_of[0], (TOKENS, D), 1.0, 6.0, ((0, 16), (1, 32))),
        "output_grad": noise(streams_of[1], (TOKENS, KW), 1.0, 6.0, ((0, 512),)),
        "key_weight": noise(streams_of[2], (D, KW), D ** -0.5, 0.0625, ((0, 32),)),
        "adapter_down": noise(streams_of[3], (ADAPTERS, R, D), D ** -0.5, 0.0625, ((0, 16), (2, 32))),
        "adapter_up": noise(streams_of[4], (ADAPTERS, R, KW), KW ** -0.5, 0.1875, ((0, 16), (2, 32))),
        "segment_adapter": place_ends(skewed_ids(streams_of[5], (SEGS,), ADAPTERS, 2), jax.random.fold_in(streams_of[5], 3), 0, ADAPTERS - 1).astype(jnp.int32),
        "adapter_slot": jax.random.permutation(streams_of[6], ADAPTERS).astype(jnp.int32),
        "live_segments": draw_live_segments(jax.random.fold_in(streams_of[8], 71), 0),
    }


def reference(layer_input, output_grad, key_weight, adapter_down, adapter_up, segment_adapter, adapter_slot, live_segments):
    seg_slot = jnp.take(adapter_slot, segment_adapter, axis=0).astype(jnp.int32)
    positions = jnp.arange(SEGS_GROUP, dtype=jnp.int32)
    slot_ids = jnp.arange(ADAPTERS, dtype=jnp.int32)

    def one_group(totals, inputs):
        input_rows, grad_rows, slots, count = inputs
        live = (positions < count).astype(grad_rows.dtype)
        masked = grad_rows.reshape(SEGS_GROUP, SEG, KW) * live[:, None, None]
        down_seg = jnp.take(adapter_down, slots, axis=0).astype(jnp.float32)
        up_seg = jnp.take(adapter_up, slots, axis=0).astype(jnp.float32)
        masked_wide = masked.astype(jnp.float32)
        input_wide = input_rows.reshape(SEGS_GROUP, SEG, D).astype(jnp.float32)
        lowrank = jnp.einsum("sjk,srk->sjr", masked_wide, up_seg).astype(jnp.bfloat16)
        projected = jnp.einsum("sjd,srd->sjr", input_wide, down_seg).astype(jnp.bfloat16)
        frozen = jnp.dot(masked.reshape(TOK_GROUP, KW), key_weight.T, preferred_element_type=jnp.float32)
        extra = 2.0 * jnp.einsum("sjr,srd->sjd", lowrank.astype(jnp.float32), down_seg)
        input_grad = (frozen + extra.reshape(TOK_GROUP, D)).astype(jnp.bfloat16)
        seg_down = 2.0 * jnp.einsum("sjr,sjd->srd", lowrank.astype(jnp.float32), input_wide)
        seg_up = 2.0 * jnp.einsum("sjr,sjk->srk", projected.astype(jnp.float32), masked_wide)
        onehot = (slots[:, None] == slot_ids[None, :]).astype(jnp.float32)
        part_down = jnp.einsum("sa,srd->ard", onehot, seg_down, precision=lax.Precision.HIGHEST).astype(jnp.bfloat16)
        part_up = jnp.einsum("sa,srk->ark", onehot, seg_up, precision=lax.Precision.HIGHEST).astype(jnp.bfloat16)
        totals = (totals[0] + part_down.astype(jnp.float32), totals[1] + part_up.astype(jnp.float32))
        return totals, input_grad

    inputs = (layer_input.reshape(N_DP, TOK_GROUP, D), output_grad.reshape(N_DP, TOK_GROUP, KW), seg_slot.reshape(N_DP, SEGS_GROUP), live_segments)
    start = (jnp.zeros((ADAPTERS, R, D), jnp.float32), jnp.zeros((ADAPTERS, R, KW), jnp.float32))
    totals, input_grad = lax.scan(one_group, start, inputs)
    return input_grad.reshape(TOKENS, D), totals[0].astype(jnp.bfloat16), totals[1].astype(jnp.bfloat16)
```

```python
import jax
import jax.numpy as jnp
from jax import lax
from jax.sharding import PartitionSpec as P


def on_device(
    layer_input,
    output_grad,
    key_weight,
    adapter_down,
    adapter_up,
    segment_adapter,
    adapter_slot,
    live_segments,
):
    tensor_size = lax.axis_size("tensor")
    position = lax.axis_index("tensor")
    group_count = lax.axis_size("dp")
    group_index = lax.axis_index("dp")
    tok_group = layer_input.shape[0]
    width_shard = layer_input.shape[1]
    key_width = output_grad.shape[1]
    key_shard = key_width // tensor_size
    adapters = adapter_slot.shape[0]
    rank_dim = adapter_down.shape[1]
    seg_total = segment_adapter.shape[0]
    seg_group = seg_total // group_count
    seg_len = tok_group // seg_group

    whole_raw = lax.all_gather(output_grad, "tensor", axis=0, tiled=True)

    slot_ids = jnp.arange(adapters, dtype=jnp.int32)
    lookup = segment_adapter[:, None] == slot_ids[None, :]
    every_slot = jnp.sum(jnp.where(lookup, adapter_slot[None, :], 0), axis=1)
    seg_slot = lax.dynamic_slice_in_dim(every_slot, group_index * seg_group, seg_group)
    seg_live = jnp.arange(seg_group, dtype=jnp.int32) < live_segments[0]

    local_store = jnp.concatenate([adapter_down, adapter_up], axis=2)
    stores = lax.all_gather(local_store, "dp", axis=0, tiled=True)
    choose = (seg_slot[:, None] == slot_ids[None, :]).astype(jnp.bfloat16)
    seg_store = jnp.dot(choose, stores.reshape(adapters, -1), preferred_element_type=jnp.float32)
    seg_store = seg_store.astype(jnp.bfloat16).reshape(seg_group, rank_dim, width_shard + key_shard)
    down_seg = seg_store[:, :, :width_shard]
    up_seg = seg_store[:, :, width_shard:]

    whole = jnp.where(
        jnp.repeat(seg_live, seg_len)[:, None], whole_raw, jnp.zeros_like(whole_raw)
    )
    own_keys = lax.dynamic_slice_in_dim(whole, position * key_shard, key_shard, 1).reshape(
        seg_group, seg_len, key_shard
    )
    input_seg = layer_input.reshape(seg_group, seg_len, width_shard)
    up_part = jnp.einsum("sjk,srk->srj", own_keys, up_seg, preferred_element_type=jnp.float32)
    down_part = jnp.einsum("sjd,srd->srj", input_seg, down_seg, preferred_element_type=jnp.float32)
    both = lax.psum(jnp.stack([up_part, down_part]), "tensor")
    both = lax.reduce_precision(both, exponent_bits=8, mantissa_bits=7)
    lowrank = both[0].astype(jnp.bfloat16)
    projected = both[1].astype(jnp.bfloat16)

    frozen = lax.dot_general(
        whole, key_weight, (((1,), (1,)), ((), ())), preferred_element_type=jnp.float32
    )
    extra = jnp.einsum("srj,srd->sjd", lowrank, down_seg, preferred_element_type=jnp.float32)
    input_grad = (frozen + 2.0 * extra.reshape(tok_group, width_shard)).astype(jnp.bfloat16)

    seg_down = 2.0 * jnp.einsum(
        "srj,sjd->srd", lowrank, input_seg, preferred_element_type=jnp.float32
    )
    seg_up = 2.0 * jnp.einsum(
        "srj,sjk->srk", projected, own_keys, preferred_element_type=jnp.float32
    )
    seg_grad = jnp.concatenate([seg_down, seg_up], axis=2)
    onehot = (seg_slot[:, None] == slot_ids[None, :]).astype(jnp.float32)
    part = jnp.einsum("sa,srd->ard", onehot, seg_grad, precision=lax.Precision.HIGHEST)
    part = lax.reduce_precision(part, exponent_bits=8, mantissa_bits=7)
    total = lax.psum_scatter(part, "dp", scatter_dimension=0, tiled=True)
    down_grad = total[:, :, :width_shard].astype(jnp.bfloat16)
    up_grad = total[:, :, width_shard:].astype(jnp.bfloat16)
    return (input_grad, down_grad, up_grad)


def solution(mesh):
    in_specs = (
        P("dp", "tensor"),
        P(("dp", "tensor"), None),
        P("tensor", None),
        P("dp", None, "tensor"),
        P("dp", None, "tensor"),
        P(),
        P(),
        P("dp"),
    )
    out_specs = (P("dp", "tensor"), P("dp", None, "tensor"), P("dp", None, "tensor"))
    return jax.shard_map(
        on_device, mesh=mesh, in_specs=in_specs, out_specs=out_specs, check_vma=False
    )
```

```python
import jax
import jax.numpy as jnp
from jax import lax
from jax.sharding import PartitionSpec as P


def on_device(
    layer_input,
    output_grad,
    key_weight,
    adapter_down,
    adapter_up,
    segment_adapter,
    adapter_slot,
    live_segments,
):
    tensor_size = lax.axis_size("tensor")
    position = lax.axis_index("tensor")
    group_count = lax.axis_size("dp")
    group_index = lax.axis_index("dp")
    row_count = output_grad.shape[0]
    tok_group = layer_input.shape[0]
    width_shard = layer_input.shape[1]
    key_width = output_grad.shape[1]
    key_shard = key_width // tensor_size
    adapters = adapter_slot.shape[0]
    rank_dim = adapter_down.shape[1]
    per_owner = adapter_down.shape[0]
    seg_total = segment_adapter.shape[0]
    seg_group = seg_total // group_count
    seg_len = tok_group // seg_group
    f32 = jnp.float32
    bf16 = jnp.bfloat16

    whole_raw = lax.all_gather(output_grad, "tensor", axis=0, tiled=True)

    slot_ids = jnp.arange(adapters, dtype=jnp.int32)
    lookup = segment_adapter[:, None] == slot_ids[None, :]
    every_slot = jnp.sum(jnp.where(lookup, adapter_slot[None, :], 0), axis=1)
    seg_slot = lax.dynamic_slice_in_dim(every_slot, group_index * seg_group, seg_group)
    seg_live = jnp.arange(seg_group, dtype=jnp.int32) < live_segments[0]

    local_store = jnp.concatenate([adapter_down, adapter_up], axis=2)
    spread = jnp.broadcast_to(local_store[None], (group_count,) + local_store.shape)
    stores = lax.all_to_all(spread, "dp", 0, 0, tiled=True).reshape(adapters, -1)
    choose = (seg_slot[:, None] == slot_ids[None, :]).astype(bf16)
    seg_store = jnp.dot(choose, stores, preferred_element_type=f32).astype(bf16)
    seg_store = seg_store.reshape(seg_group, rank_dim, width_shard + key_shard)
    down_seg = seg_store[:, :, :width_shard]
    up_seg = seg_store[:, :, width_shard:]

    input_seg = layer_input.reshape(seg_group, seg_len, width_shard)
    proj_part = jnp.einsum("sjd,srd->srj", input_seg, down_seg, preferred_element_type=f32)
    first = jnp.concatenate([proj_part, up_seg.astype(f32)], axis=2)
    first = lax.all_to_all(first, "tensor", 0, 0, tiled=True)
    projected_own = jnp.sum(first[:, :, :seg_len], axis=0).astype(bf16)
    up_own = jnp.transpose(first[:, :, seg_len:], (1, 0, 2)).reshape(rank_dim, key_width)
    up_own = up_own.astype(bf16)

    own_live = position < live_segments[0]
    masked_own = jnp.where(own_live, output_grad, jnp.zeros_like(output_grad))
    lowrank_own = lax.dot_general(
        masked_own, up_own, (((1,), (1,)), ((), ())), preferred_element_type=f32
    ).astype(bf16)
    seg_up_own = 2.0 * jnp.dot(projected_own, masked_own, preferred_element_type=f32)

    low_spread = jnp.broadcast_to(
        lowrank_own.astype(f32).reshape(1, row_count * rank_dim),
        (tensor_size, row_count * rank_dim),
    )
    up_pieces = jnp.transpose(
        seg_up_own.reshape(rank_dim, tensor_size, key_shard), (1, 0, 2)
    ).reshape(tensor_size, rank_dim * key_shard)
    second = jnp.concatenate([low_spread, up_pieces], axis=1)
    second = lax.all_to_all(second, "tensor", 0, 0, tiled=True)
    lowrank = second[:, : row_count * rank_dim].reshape(seg_group, seg_len, rank_dim)
    lowrank = lowrank.astype(bf16)
    seg_up = second[:, row_count * rank_dim :].reshape(seg_group, rank_dim, key_shard)

    seg_down = 2.0 * jnp.einsum("sjr,sjd->srd", lowrank, input_seg, preferred_element_type=f32)
    seg_grad = jnp.concatenate([seg_down, seg_up], axis=2)
    onehot = (seg_slot[:, None] == slot_ids[None, :]).astype(f32)
    part = jnp.einsum("sa,srd->ard", onehot, seg_grad, precision=lax.Precision.HIGHEST)
    part = part.astype(bf16).reshape(group_count, per_owner, rank_dim, -1)
    gathered = lax.all_to_all(part, "dp", 0, 0, tiled=True)
    total = jnp.sum(gathered.astype(f32), axis=0)
    down_grad = total[:, :, :width_shard].astype(bf16)
    up_grad = total[:, :, width_shard:].astype(bf16)

    whole = jnp.where(
        jnp.repeat(seg_live, seg_len)[:, None], whole_raw, jnp.zeros_like(whole_raw)
    )
    frozen = lax.dot_general(
        whole, key_weight, (((1,), (1,)), ((), ())), preferred_element_type=f32
    )
    extra = jnp.einsum("sjr,srd->sjd", lowrank, down_seg, preferred_element_type=f32)
    input_grad = (frozen + 2.0 * extra.reshape(tok_group, width_shard)).astype(bf16)
    return (input_grad, down_grad, up_grad)


def solution(mesh):
    in_specs = (
        P("dp", "tensor"),
        P(("dp", "tensor"), None),
        P("tensor", None),
        P("dp", None, "tensor"),
        P("dp", None, "tensor"),
        P(),
        P(),
        P("dp"),
    )
    out_specs = (P("dp", "tensor"), P("dp", None, "tensor"), P("dp", None, "tensor"))
    return jax.shard_map(
        on_device, mesh=mesh, in_specs=in_specs, out_specs=out_specs, check_vma=False
    )
```

```python
import jax
import jax.numpy as jnp
from jax import lax
from jax.sharding import PartitionSpec as P


def on_device(
    layer_input,
    output_grad,
    key_weight,
    adapter_down,
    adapter_up,
    segment_adapter,
    adapter_slot,
    live_segments,
):
    tensor_size = lax.axis_size("tensor")
    position = lax.axis_index("tensor")
    group_count = lax.axis_size("dp")
    group_index = lax.axis_index("dp")
    row_count = output_grad.shape[0]
    tok_group = layer_input.shape[0]
    width_shard = layer_input.shape[1]
    key_width = output_grad.shape[1]
    key_shard = key_width // tensor_size
    adapters = adapter_slot.shape[0]
    rank_dim = adapter_down.shape[1]
    per_owner = adapter_down.shape[0]
    seg_total = segment_adapter.shape[0]
    seg_group = seg_total // group_count
    seg_len = tok_group // seg_group
    f32 = jnp.float32
    bf16 = jnp.bfloat16

    whole_raw = lax.all_gather(output_grad, "tensor", axis=0, tiled=True)

    slot_ids = jnp.arange(adapters, dtype=jnp.int32)
    lookup = segment_adapter[:, None] == slot_ids[None, :]
    every_slot = jnp.sum(jnp.where(lookup, adapter_slot[None, :], 0), axis=1)
    seg_slot = lax.dynamic_slice_in_dim(every_slot, group_index * seg_group, seg_group)
    seg_live = jnp.arange(seg_group, dtype=jnp.int32) < live_segments[0]

    local_store = jnp.concatenate([adapter_down, adapter_up], axis=2)
    spread = jnp.broadcast_to(local_store[None], (group_count,) + local_store.shape)
    stores = lax.all_to_all(spread, "dp", 0, 0, tiled=True)
    stores = stores.reshape((adapters,) + local_store.shape[1:])
    choose = (seg_slot[:, None] == slot_ids[None, :]).astype(bf16)
    seg_store = jnp.einsum("sa,ark->srk", choose, stores, preferred_element_type=f32)
    seg_store = seg_store.astype(bf16)
    down_seg = seg_store[:, :, :width_shard]
    up_seg = seg_store[:, :, width_shard:]

    input_seg = layer_input.reshape(seg_group, seg_len, width_shard)
    proj_part = jnp.einsum("sjd,srd->srj", input_seg, down_seg, preferred_element_type=f32)
    first = jnp.concatenate([proj_part, up_seg.astype(f32)], axis=2)
    first = lax.all_to_all(first, "tensor", 0, 0, tiled=True)
    projected_own = jnp.sum(first[:, :, :seg_len], axis=0).astype(bf16)
    up_own = jnp.transpose(first[:, :, seg_len:], (1, 0, 2)).reshape(rank_dim, key_width)
    up_own = up_own.astype(bf16)

    own_live = position < live_segments[0]
    masked_own = jnp.where(own_live, output_grad, jnp.zeros_like(output_grad))
    lowrank_own = lax.dot_general(
        masked_own, up_own, (((1,), (1,)), ((), ())), preferred_element_type=f32
    ).astype(bf16)
    seg_up_own = 2.0 * jnp.dot(projected_own, masked_own, preferred_element_type=f32)

    low_spread = jnp.broadcast_to(
        lowrank_own.reshape(1, row_count * rank_dim), (tensor_size, row_count * rank_dim)
    )
    up_pieces = jnp.transpose(
        seg_up_own.reshape(rank_dim, tensor_size, key_shard), (1, 0, 2)
    ).reshape(tensor_size, rank_dim * key_shard)
    up_high = up_pieces.astype(bf16)
    up_low = (up_pieces - up_high.astype(f32)).astype(bf16)
    second = jnp.concatenate([low_spread, up_high, up_low], axis=1)
    second = second.reshape(tensor_size, -1, 128)
    second = lax.all_to_all(second, "tensor", 0, 0, tiled=True).reshape(tensor_size, -1)
    lowrank = second[:, : row_count * rank_dim].reshape(seg_group, seg_len, rank_dim)
    piece = rank_dim * key_shard
    low_end = row_count * rank_dim
    seg_up = second[:, low_end : low_end + piece].astype(f32)
    seg_up = seg_up + second[:, low_end + piece :].astype(f32)
    seg_up = seg_up.reshape(seg_group, rank_dim, key_shard)

    seg_down = 2.0 * jnp.einsum("sjr,sjd->srd", lowrank, input_seg, preferred_element_type=f32)
    seg_grad = jnp.concatenate([seg_down, seg_up], axis=2)
    onehot = (seg_slot[:, None] == slot_ids[None, :]).astype(f32)
    part = jnp.einsum("sa,srd->ard", onehot, seg_grad, precision=lax.Precision.HIGHEST)
    part = part.astype(bf16).reshape(group_count, per_owner, rank_dim, -1)
    gathered = lax.all_to_all(part, "dp", 0, 0, tiled=True)
    total = jnp.sum(gathered.astype(f32), axis=0)
    down_grad = total[:, :, :width_shard].astype(bf16)
    up_grad = total[:, :, width_shard:].astype(bf16)

    whole = jnp.where(
        jnp.repeat(seg_live, seg_len)[:, None], whole_raw, jnp.zeros_like(whole_raw)
    )
    frozen = lax.dot_general(
        whole, key_weight, (((1,), (1,)), ((), ())), preferred_element_type=f32
    )
    extra = jnp.einsum("sjr,srd->sjd", lowrank, down_seg, preferred_element_type=f32)
    input_grad = (frozen + 2.0 * extra.reshape(tok_group, width_shard)).astype(bf16)
    return (input_grad, down_grad, up_grad)


def solution(mesh):
    in_specs = (
        P("dp", "tensor"),
        P(("dp", "tensor"), None),
        P("tensor", None),
        P("dp", None, "tensor"),
        P("dp", None, "tensor"),
        P(),
        P(),
        P("dp"),
    )
    out_specs = (P("dp", "tensor"), P("dp", None, "tensor"), P("dp", None, "tensor"))
    return jax.shard_map(
        on_device, mesh=mesh, in_specs=in_specs, out_specs=out_specs, check_vma=False
    )
```

```python
import jax
import jax.numpy as jnp
from jax import lax
from jax.sharding import PartitionSpec as P


def on_device(
    layer_input,
    output_grad,
    key_weight,
    adapter_down,
    adapter_up,
    segment_adapter,
    adapter_slot,
    live_segments,
):
    tensor_size = lax.axis_size("tensor")
    position = lax.axis_index("tensor")
    group_count = lax.axis_size("dp")
    group_index = lax.axis_index("dp")
    row_count = output_grad.shape[0]
    tok_group = layer_input.shape[0]
    width_shard = layer_input.shape[1]
    key_width = output_grad.shape[1]
    key_shard = key_width // tensor_size
    adapters = adapter_slot.shape[0]
    rank_dim = adapter_down.shape[1]
    per_owner = adapter_down.shape[0]
    seg_total = segment_adapter.shape[0]
    seg_group = seg_total // group_count
    seg_len = tok_group // seg_group
    f32 = jnp.float32
    bf16 = jnp.bfloat16

    whole_raw = lax.all_gather(output_grad, "tensor", axis=0, tiled=True)

    slot_ids = jnp.arange(adapters, dtype=jnp.int32)
    lookup = segment_adapter[:, None] == slot_ids[None, :]
    every_slot = jnp.sum(jnp.where(lookup, adapter_slot[None, :], 0), axis=1)
    seg_slot = lax.dynamic_slice_in_dim(every_slot, group_index * seg_group, seg_group)
    seg_live = jnp.arange(seg_group, dtype=jnp.int32) < live_segments[0]

    local_store = jnp.concatenate([adapter_down, adapter_up], axis=2)
    spread = jnp.broadcast_to(local_store[None], (group_count,) + local_store.shape)
    stores = lax.all_to_all(spread, "dp", 0, 0, tiled=True)
    stores = stores.reshape((adapters,) + local_store.shape[1:])
    choose = (seg_slot[:, None] == slot_ids[None, :]).astype(bf16)
    seg_store = jnp.einsum("sa,ark->srk", choose, stores, preferred_element_type=f32)
    seg_store = seg_store.astype(bf16)
    down_seg = seg_store[:, :, :width_shard]
    up_seg = seg_store[:, :, width_shard:]

    input_seg = layer_input.reshape(seg_group, seg_len, width_shard)
    proj_part = jnp.einsum("sjd,srd->srj", input_seg, down_seg, preferred_element_type=f32)
    first = jnp.concatenate([proj_part, up_seg.astype(f32)], axis=2)
    first = lax.all_to_all(first, "tensor", 0, 0, tiled=True)
    projected_own = jnp.sum(first[:, :, :seg_len], axis=0).astype(bf16)
    up_own = jnp.transpose(first[:, :, seg_len:], (1, 0, 2)).reshape(rank_dim, key_width)
    up_own = up_own.astype(bf16)

    own_live = position < live_segments[0]
    masked_own = jnp.where(own_live, output_grad, jnp.zeros_like(output_grad))
    lowrank_own = lax.dot_general(
        masked_own, up_own, (((1,), (1,)), ((), ())), preferred_element_type=f32
    ).astype(bf16)
    seg_up_own = 2.0 * jnp.dot(projected_own, masked_own, preferred_element_type=f32)

    low_spread = jnp.broadcast_to(
        lowrank_own.reshape(1, row_count * rank_dim), (tensor_size, row_count * rank_dim)
    )
    up_pieces = jnp.transpose(
        seg_up_own.reshape(rank_dim, tensor_size, key_shard), (1, 0, 2)
    ).reshape(tensor_size, rank_dim * key_shard)
    up_round = lax.reduce_precision(up_pieces, exponent_bits=8, mantissa_bits=7)
    up_high = up_round.astype(bf16)
    up_low = (up_pieces - up_round).astype(bf16)
    second = jnp.concatenate([low_spread, up_high, up_low], axis=1)
    second = second.reshape(tensor_size, -1, 128)
    second = lax.all_to_all(second, "tensor", 0, 0, tiled=True).reshape(tensor_size, -1)
    lowrank = second[:, : row_count * rank_dim].reshape(seg_group, seg_len, rank_dim)
    piece = rank_dim * key_shard
    low_end = row_count * rank_dim
    seg_up = second[:, low_end : low_end + piece].astype(f32)
    seg_up = seg_up + second[:, low_end + piece :].astype(f32)
    seg_up = seg_up.reshape(seg_group, rank_dim, key_shard)

    seg_down = 2.0 * jnp.einsum("sjr,sjd->srd", lowrank, input_seg, preferred_element_type=f32)
    seg_grad = jnp.concatenate([seg_down, seg_up], axis=2)
    onehot = (seg_slot[:, None] == slot_ids[None, :]).astype(f32)
    part = jnp.einsum("sa,srd->ard", onehot, seg_grad, precision=lax.Precision.HIGHEST)
    part = part.astype(bf16).reshape(group_count, per_owner, rank_dim, -1)
    gathered = lax.all_to_all(part, "dp", 0, 0, tiled=True)
    whole = jnp.where(
        jnp.repeat(seg_live, seg_len)[:, None], whole_raw, jnp.zeros_like(whole_raw)
    )
    frozen = lax.dot_general(
        whole, key_weight, (((1,), (1,)), ((), ())), preferred_element_type=f32
    )
    extra = jnp.einsum("sjr,srd->sjd", lowrank, down_seg, preferred_element_type=f32)
    input_grad = (frozen + 2.0 * extra.reshape(tok_group, width_shard)).astype(bf16)
    gathered, input_grad = lax.optimization_barrier((gathered, input_grad))
    total = jnp.sum(gathered.astype(f32), axis=0)
    down_grad = total[:, :, :width_shard].astype(bf16)
    up_grad = total[:, :, width_shard:].astype(bf16)

    return (input_grad, down_grad, up_grad)


def solution(mesh):
    in_specs = (
        P("dp", "tensor"),
        P(("dp", "tensor"), None),
        P("tensor", None),
        P("dp", None, "tensor"),
        P("dp", None, "tensor"),
        P(),
        P(),
        P("dp"),
    )
    out_specs = (P("dp", "tensor"), P("dp", None, "tensor"), P("dp", None, "tensor"))
    return jax.shard_map(
        on_device, mesh=mesh, in_specs=in_specs, out_specs=out_specs, check_vma=False
    )
```

```python
import jax
import jax.numpy as jnp
from jax import lax
from jax.sharding import PartitionSpec as P


def on_device(
    layer_input,
    output_grad,
    key_weight,
    adapter_down,
    adapter_up,
    segment_adapter,
    adapter_slot,
    live_segments,
):
    tensor_size = lax.axis_size("tensor")
    position = lax.axis_index("tensor")
    group_count = lax.axis_size("dp")
    group_index = lax.axis_index("dp")
    row_count = output_grad.shape[0]
    tok_group = layer_input.shape[0]
    width_shard = layer_input.shape[1]
    key_width = output_grad.shape[1]
    key_shard = key_width // tensor_size
    adapters = adapter_slot.shape[0]
    rank_dim = adapter_down.shape[1]
    per_owner = adapter_down.shape[0]
    seg_total = segment_adapter.shape[0]
    seg_group = seg_total // group_count
    seg_len = tok_group // seg_group
    f32 = jnp.float32
    bf16 = jnp.bfloat16

    whole_raw = lax.all_gather(output_grad, "tensor", axis=0, tiled=True)

    slot_ids = jnp.arange(adapters, dtype=jnp.int32)
    lookup = segment_adapter[:, None] == slot_ids[None, :]
    every_slot = jnp.sum(jnp.where(lookup, adapter_slot[None, :], 0), axis=1)
    seg_slot = lax.dynamic_slice_in_dim(every_slot, group_index * seg_group, seg_group)
    seg_live = jnp.arange(seg_group, dtype=jnp.int32) < live_segments[0]

    local_store = jnp.concatenate([adapter_down, adapter_up], axis=2)
    spread = jnp.broadcast_to(local_store[None], (group_count,) + local_store.shape)
    stores = lax.all_to_all(spread, "dp", 0, 0, tiled=True)
    stores = stores.reshape((adapters,) + local_store.shape[1:])
    choose = (seg_slot[:, None] == slot_ids[None, :]).astype(bf16)
    seg_store = jnp.einsum("sa,ark->srk", choose, stores, preferred_element_type=f32)
    seg_store = seg_store.astype(bf16)
    down_seg = seg_store[:, :, :width_shard]
    up_seg = seg_store[:, :, width_shard:]

    input_seg = layer_input.reshape(seg_group, seg_len, width_shard)
    proj_part = jnp.einsum("sjd,srd->srj", input_seg, down_seg, preferred_element_type=f32)
    first = jnp.concatenate([proj_part, up_seg.astype(f32)], axis=2)
    first = lax.all_to_all(first, "tensor", 0, 0, tiled=True)
    projected_own = jnp.sum(first[:, :, :seg_len], axis=0).astype(bf16)
    up_own = jnp.transpose(first[:, :, seg_len:], (1, 0, 2)).reshape(rank_dim, key_width)
    up_own = up_own.astype(bf16)

    own_live = position < live_segments[0]
    masked_own = jnp.where(own_live, output_grad, jnp.zeros_like(output_grad))
    lowrank_own = lax.dot_general(
        masked_own, up_own, (((1,), (1,)), ((), ())), preferred_element_type=f32
    ).astype(bf16)
    seg_up_own = 2.0 * jnp.dot(projected_own, masked_own, preferred_element_type=f32)

    low_spread = jnp.broadcast_to(
        lowrank_own.reshape(1, row_count * rank_dim), (tensor_size, row_count * rank_dim)
    )
    up_pieces = jnp.transpose(
        seg_up_own.reshape(rank_dim, tensor_size, key_shard), (1, 0, 2)
    ).reshape(tensor_size, rank_dim * key_shard)
    up_round = lax.reduce_precision(up_pieces, exponent_bits=8, mantissa_bits=7)
    up_high = up_round.astype(bf16)
    up_low = (up_pieces - up_round).astype(bf16)
    second = jnp.concatenate([low_spread, up_high, up_low], axis=1)
    second = second.reshape(tensor_size, -1, 128)
    second = lax.all_to_all(second, "tensor", 0, 0, tiled=True).reshape(tensor_size, -1)
    lowrank = second[:, : row_count * rank_dim].reshape(seg_group, seg_len, rank_dim)
    piece = rank_dim * key_shard
    low_end = row_count * rank_dim
    seg_up = second[:, low_end : low_end + piece].astype(f32)
    seg_up = seg_up + second[:, low_end + piece :].astype(f32)
    seg_up = seg_up.reshape(seg_group, rank_dim, key_shard)

    seg_down = 2.0 * jnp.einsum("sjr,sjd->srd", lowrank, input_seg, preferred_element_type=f32)
    seg_grad = jnp.concatenate([seg_down, seg_up], axis=2)
    onehot = (slot_ids[:, None] == seg_slot[None, :]).astype(bf16)
    grad_round = lax.reduce_precision(seg_grad, exponent_bits=8, mantissa_bits=7)
    grad_high = grad_round.astype(bf16)
    grad_low = (seg_grad - grad_round).astype(bf16)
    part = jnp.einsum("as,srd->ard", onehot, grad_high, preferred_element_type=f32)
    part = part + jnp.einsum("as,srd->ard", onehot, grad_low, preferred_element_type=f32)
    part = part.astype(bf16).reshape(group_count, per_owner, rank_dim, -1)
    gathered = lax.all_to_all(part, "dp", 0, 0, tiled=True)
    whole = jnp.where(
        jnp.repeat(seg_live, seg_len)[:, None], whole_raw, jnp.zeros_like(whole_raw)
    )
    frozen = lax.dot_general(
        whole, key_weight, (((1,), (1,)), ((), ())), preferred_element_type=f32
    )
    extra = jnp.einsum("sjr,srd->sjd", lowrank, down_seg, preferred_element_type=f32)
    input_grad = (frozen + 2.0 * extra.reshape(tok_group, width_shard)).astype(bf16)
    gathered, input_grad = lax.optimization_barrier((gathered, input_grad))
    down_grad = jnp.sum(gathered[..., :width_shard].astype(f32), axis=0).astype(bf16)
    up_grad = jnp.sum(gathered[..., width_shard:].astype(f32), axis=0).astype(bf16)

    return (input_grad, down_grad, up_grad)


def solution(mesh):
    in_specs = (
        P("dp", "tensor"),
        P(("dp", "tensor"), None),
        P("tensor", None),
        P("dp", None, "tensor"),
        P("dp", None, "tensor"),
        P(),
        P(),
        P("dp"),
    )
    out_specs = (P("dp", "tensor"), P("dp", None, "tensor"), P("dp", None, "tensor"))
    return jax.shard_map(
        on_device, mesh=mesh, in_specs=in_specs, out_specs=out_specs, check_vma=False
    )
```

```python
import jax
import jax.numpy as jnp
from jax import lax
from jax.sharding import PartitionSpec as P


def on_device(
    layer_input,
    output_grad,
    key_weight,
    adapter_down,
    adapter_up,
    segment_adapter,
    adapter_slot,
    live_segments,
):
    tensor_size = lax.axis_size("tensor")
    position = lax.axis_index("tensor")
    group_count = lax.axis_size("dp")
    group_index = lax.axis_index("dp")
    row_count = output_grad.shape[0]
    tok_group = layer_input.shape[0]
    width_shard = layer_input.shape[1]
    key_width = output_grad.shape[1]
    key_shard = key_width // tensor_size
    adapters = adapter_slot.shape[0]
    rank_dim = adapter_down.shape[1]
    per_owner = adapter_down.shape[0]
    seg_total = segment_adapter.shape[0]
    seg_group = seg_total // group_count
    seg_len = tok_group // seg_group
    f32 = jnp.float32
    bf16 = jnp.bfloat16

    whole_raw = lax.all_gather(output_grad, "tensor", axis=0, tiled=True)

    slot_ids = jnp.arange(adapters, dtype=jnp.int32)
    lookup = segment_adapter[:, None] == slot_ids[None, :]
    every_slot = jnp.sum(jnp.where(lookup, adapter_slot[None, :], 0), axis=1)
    seg_slot = lax.dynamic_slice_in_dim(every_slot, group_index * seg_group, seg_group)
    seg_live = jnp.arange(seg_group, dtype=jnp.int32) < live_segments[0]

    local_store = jnp.concatenate([adapter_down, adapter_up], axis=2)
    spread = jnp.broadcast_to(local_store[None], (group_count,) + local_store.shape)
    stores = lax.all_to_all(spread, "dp", 0, 0, tiled=True)
    stores = stores.reshape((adapters,) + local_store.shape[1:])
    choose = (seg_slot[:, None] == slot_ids[None, :]).astype(bf16)
    seg_store = jnp.einsum("sa,ark->srk", choose, stores, preferred_element_type=f32)
    seg_store = seg_store.astype(bf16)
    down_seg = seg_store[:, :, :width_shard]
    up_seg = seg_store[:, :, width_shard:]

    input_seg = layer_input.reshape(seg_group, seg_len, width_shard)
    proj_part = jnp.einsum("sjd,srd->srj", input_seg, down_seg, preferred_element_type=f32)
    first = jnp.concatenate([proj_part, up_seg.astype(f32)], axis=2)
    first = lax.all_to_all(first, "tensor", 0, 0, tiled=True)
    projected_own = jnp.sum(first[:, :, :seg_len], axis=0).astype(bf16)
    up_own = jnp.transpose(first[:, :, seg_len:], (1, 0, 2)).reshape(rank_dim, key_width)
    up_own = up_own.astype(bf16)

    own_live = position < live_segments[0]
    masked_own = jnp.where(own_live, output_grad, jnp.zeros_like(output_grad))
    lowrank_own = lax.dot_general(
        masked_own, up_own, (((1,), (1,)), ((), ())), preferred_element_type=f32
    ).astype(bf16)
    seg_up_own = 2.0 * jnp.dot(projected_own, masked_own, preferred_element_type=f32)

    low_spread = jnp.broadcast_to(
        lowrank_own.reshape(1, row_count * rank_dim), (tensor_size, row_count * rank_dim)
    )
    up_pieces = jnp.transpose(
        seg_up_own.reshape(rank_dim, tensor_size, key_shard), (1, 0, 2)
    ).reshape(tensor_size, rank_dim * key_shard)
    up_round = lax.reduce_precision(up_pieces, exponent_bits=8, mantissa_bits=7)
    up_high = up_round.astype(bf16)
    up_low = (up_pieces - up_round).astype(bf16)
    second = jnp.concatenate([low_spread, up_high, up_low], axis=1)
    second = second.reshape(tensor_size, -1, 128)
    second = lax.all_to_all(second, "tensor", 0, 0, tiled=True).reshape(tensor_size, -1)
    lowrank = second[:, : row_count * rank_dim].reshape(seg_group, seg_len, rank_dim)
    piece = rank_dim * key_shard
    low_end = row_count * rank_dim
    seg_up = second[:, low_end : low_end + piece].astype(f32)
    seg_up = seg_up + second[:, low_end + piece :].astype(f32)
    seg_up = seg_up.reshape(seg_group, rank_dim, key_shard)

    seg_down = 2.0 * jnp.einsum("sjr,sjd->srd", lowrank, input_seg, preferred_element_type=f32)
    seg_grad = jnp.concatenate([seg_down, seg_up], axis=2)
    onehot = (slot_ids[:, None] == seg_slot[None, :]).astype(bf16)
    grad_round = lax.reduce_precision(seg_grad, exponent_bits=8, mantissa_bits=7)
    grad_high = grad_round.astype(bf16)
    grad_low = (seg_grad - grad_round).astype(bf16)
    flat_high = grad_high.reshape(seg_group, -1)
    flat_low = grad_low.reshape(seg_group, -1)
    part = jnp.dot(onehot, flat_high, preferred_element_type=f32)
    part = part + jnp.dot(onehot, flat_low, preferred_element_type=f32)
    part = part.astype(bf16).reshape(group_count, per_owner, -1)
    gathered = lax.all_to_all(part, "dp", 0, 0, tiled=True)
    whole = jnp.where(
        jnp.repeat(seg_live, seg_len)[:, None], whole_raw, jnp.zeros_like(whole_raw)
    )
    frozen = lax.dot_general(
        whole, key_weight, (((1,), (1,)), ((), ())), preferred_element_type=f32
    )
    extra = jnp.einsum("sjr,srd->sjd", lowrank, down_seg, preferred_element_type=f32)
    input_grad = (frozen + 2.0 * extra.reshape(tok_group, width_shard)).astype(bf16)
    gathered, input_grad = lax.optimization_barrier((gathered, input_grad))
    total = jnp.sum(gathered.astype(f32), axis=0).reshape(per_owner, rank_dim, -1)
    down_grad = total[:, :, :width_shard].astype(bf16)
    up_grad = total[:, :, width_shard:].astype(bf16)

    return (input_grad, down_grad, up_grad)


def solution(mesh):
    in_specs = (
        P("dp", "tensor"),
        P(("dp", "tensor"), None),
        P("tensor", None),
        P("dp", None, "tensor"),
        P("dp", None, "tensor"),
        P(),
        P(),
        P("dp"),
    )
    out_specs = (P("dp", "tensor"), P("dp", None, "tensor"), P("dp", None, "tensor"))
    return jax.shard_map(
        on_device, mesh=mesh, in_specs=in_specs, out_specs=out_specs, check_vma=False
    )
```

```python
import jax
import jax.numpy as jnp
from jax import lax
from jax.sharding import PartitionSpec as P


def on_device(
    layer_input,
    output_grad,
    key_weight,
    adapter_down,
    adapter_up,
    segment_adapter,
    adapter_slot,
    live_segments,
):
    tensor_size = lax.axis_size("tensor")
    position = lax.axis_index("tensor")
    group_count = lax.axis_size("dp")
    group_index = lax.axis_index("dp")
    row_count = output_grad.shape[0]
    tok_group = layer_input.shape[0]
    width_shard = layer_input.shape[1]
    key_width = output_grad.shape[1]
    key_shard = key_width // tensor_size
    adapters = adapter_slot.shape[0]
    rank_dim = adapter_down.shape[1]
    per_owner = adapter_down.shape[0]
    seg_total = segment_adapter.shape[0]
    seg_group = seg_total // group_count
    seg_len = tok_group // seg_group
    f32 = jnp.float32
    bf16 = jnp.bfloat16

    whole_raw = lax.all_gather(output_grad, "tensor", axis=0, tiled=True)

    slot_ids = jnp.arange(adapters, dtype=jnp.int32)
    lookup = segment_adapter[:, None] == slot_ids[None, :]
    every_slot = jnp.sum(jnp.where(lookup, adapter_slot[None, :], 0), axis=1)
    seg_slot = lax.dynamic_slice_in_dim(every_slot, group_index * seg_group, seg_group)
    seg_live = jnp.arange(seg_group, dtype=jnp.int32) < live_segments[0]

    local_store = jnp.concatenate([adapter_down, adapter_up], axis=2).reshape(per_owner, -1)
    spread = jnp.broadcast_to(local_store[None], (group_count,) + local_store.shape)
    stores = lax.all_to_all(spread, "dp", 0, 0, tiled=True).reshape(adapters, -1)
    choose = (seg_slot[:, None] == slot_ids[None, :]).astype(bf16)
    seg_store = jnp.dot(choose, stores, preferred_element_type=f32).astype(bf16)
    seg_store = seg_store.reshape(seg_group, rank_dim, width_shard + key_shard)
    down_seg = seg_store[:, :, :width_shard]
    up_seg = seg_store[:, :, width_shard:]

    input_seg = layer_input.reshape(seg_group, seg_len, width_shard)
    proj_part = jnp.einsum("sjd,srd->srj", input_seg, down_seg, preferred_element_type=f32)
    first = jnp.concatenate([proj_part, up_seg.astype(f32)], axis=2).reshape(seg_group, -1)
    first = lax.all_to_all(first, "tensor", 0, 0, tiled=True)
    first = first.reshape(tensor_size, rank_dim, seg_len + key_shard)
    projected_own = jnp.sum(first[:, :, :seg_len], axis=0).astype(bf16)
    up_own = jnp.transpose(first[:, :, seg_len:], (1, 0, 2)).reshape(rank_dim, key_width)
    up_own = up_own.astype(bf16)

    own_live = position < live_segments[0]
    masked_own = jnp.where(own_live, output_grad, jnp.zeros_like(output_grad))
    lowrank_own = lax.dot_general(
        masked_own, up_own, (((1,), (1,)), ((), ())), preferred_element_type=f32
    ).astype(bf16)
    seg_up_own = 2.0 * jnp.dot(projected_own, masked_own, preferred_element_type=f32)

    low_spread = jnp.broadcast_to(
        lowrank_own.reshape(1, row_count * rank_dim), (tensor_size, row_count * rank_dim)
    )
    up_pieces = jnp.transpose(
        seg_up_own.reshape(rank_dim, tensor_size, key_shard), (1, 0, 2)
    ).reshape(tensor_size, rank_dim * key_shard)
    up_round = lax.reduce_precision(up_pieces, exponent_bits=8, mantissa_bits=7)
    up_high = up_round.astype(bf16)
    up_low = (up_pieces - up_round).astype(bf16)
    second = jnp.concatenate([low_spread, up_high, up_low], axis=1)
    second = second.reshape(tensor_size, -1, 128)
    second = lax.all_to_all(second, "tensor", 0, 0, tiled=True).reshape(tensor_size, -1)
    lowrank = second[:, : row_count * rank_dim].reshape(seg_group, seg_len, rank_dim)
    piece = rank_dim * key_shard
    low_end = row_count * rank_dim
    seg_up = second[:, low_end : low_end + piece].astype(f32)
    seg_up = seg_up + second[:, low_end + piece :].astype(f32)
    seg_up = seg_up.reshape(seg_group, rank_dim, key_shard)

    seg_down = 2.0 * jnp.einsum("sjr,sjd->srd", lowrank, input_seg, preferred_element_type=f32)
    seg_grad = jnp.concatenate([seg_down, seg_up], axis=2)
    onehot = (slot_ids[:, None] == seg_slot[None, :]).astype(bf16)
    grad_round = lax.reduce_precision(seg_grad, exponent_bits=8, mantissa_bits=7)
    grad_high = grad_round.astype(bf16)
    grad_low = (seg_grad - grad_round).astype(bf16)
    flat_high = grad_high.reshape(seg_group, -1)
    flat_low = grad_low.reshape(seg_group, -1)
    part = jnp.dot(onehot, flat_high, preferred_element_type=f32)
    part = part + jnp.dot(onehot, flat_low, preferred_element_type=f32)
    part = part.astype(bf16).reshape(group_count, per_owner, -1)
    gathered = lax.all_to_all(part, "dp", 0, 0, tiled=True)
    whole = jnp.where(
        jnp.repeat(seg_live, seg_len)[:, None], whole_raw, jnp.zeros_like(whole_raw)
    )
    frozen = lax.dot_general(
        whole, key_weight, (((1,), (1,)), ((), ())), preferred_element_type=f32
    )
    extra = jnp.einsum("sjr,srd->sjd", lowrank, down_seg, preferred_element_type=f32)
    input_grad = (frozen + 2.0 * extra.reshape(tok_group, width_shard)).astype(bf16)
    gathered, input_grad = lax.optimization_barrier((gathered, input_grad))
    total = jnp.sum(gathered.astype(f32), axis=0).reshape(per_owner, rank_dim, -1)
    down_grad = total[:, :, :width_shard].astype(bf16)
    up_grad = total[:, :, width_shard:].astype(bf16)

    return (input_grad, down_grad, up_grad)


def solution(mesh):
    in_specs = (
        P("dp", "tensor"),
        P(("dp", "tensor"), None),
        P("tensor", None),
        P("dp", None, "tensor"),
        P("dp", None, "tensor"),
        P(),
        P(),
        P("dp"),
    )
    out_specs = (P("dp", "tensor"), P("dp", None, "tensor"), P("dp", None, "tensor"))
    return jax.shard_map(
        on_device, mesh=mesh, in_specs=in_specs, out_specs=out_specs, check_vma=False
    )
```

```python
import jax
import jax.numpy as jnp
from jax import lax
from jax.sharding import PartitionSpec as P


def on_device(
    layer_input,
    output_grad,
    key_weight,
    adapter_down,
    adapter_up,
    segment_adapter,
    adapter_slot,
    live_segments,
):
    tensor_size = lax.axis_size("tensor")
    position = lax.axis_index("tensor")
    group_count = lax.axis_size("dp")
    group_index = lax.axis_index("dp")
    row_count = output_grad.shape[0]
    tok_group = layer_input.shape[0]
    width_shard = layer_input.shape[1]
    key_width = output_grad.shape[1]
    key_shard = key_width // tensor_size
    adapters = adapter_slot.shape[0]
    rank_dim = adapter_down.shape[1]
    per_owner = adapter_down.shape[0]
    seg_total = segment_adapter.shape[0]
    seg_group = seg_total // group_count
    seg_len = tok_group // seg_group
    f32 = jnp.float32
    bf16 = jnp.bfloat16

    half_key = key_width // 2
    whole_first = lax.all_gather(output_grad[:, :half_key], "tensor", axis=0, tiled=True)
    whole_second = lax.all_gather(output_grad[:, half_key:], "tensor", axis=0, tiled=True)

    slot_ids = jnp.arange(adapters, dtype=jnp.int32)
    lookup = segment_adapter[:, None] == slot_ids[None, :]
    every_slot = jnp.sum(jnp.where(lookup, adapter_slot[None, :], 0), axis=1)
    seg_slot = lax.dynamic_slice_in_dim(every_slot, group_index * seg_group, seg_group)
    seg_live = jnp.arange(seg_group, dtype=jnp.int32) < live_segments[0]

    local_store = jnp.concatenate([adapter_down, adapter_up], axis=2).reshape(per_owner, -1)
    spread = jnp.broadcast_to(local_store[None], (group_count,) + local_store.shape)
    stores = lax.all_to_all(spread, "dp", 0, 0, tiled=True).reshape(adapters, -1)
    choose = (seg_slot[:, None] == slot_ids[None, :]).astype(bf16)
    seg_store = jnp.dot(choose, stores, preferred_element_type=f32).astype(bf16)
    seg_store = seg_store.reshape(seg_group, rank_dim, width_shard + key_shard)
    down_seg = seg_store[:, :, :width_shard]
    up_seg = seg_store[:, :, width_shard:]

    input_seg = layer_input.reshape(seg_group, seg_len, width_shard)
    proj_part = jnp.einsum("sjd,srd->srj", input_seg, down_seg, preferred_element_type=f32)
    first = jnp.concatenate([proj_part, up_seg.astype(f32)], axis=2).reshape(seg_group, -1)
    first = lax.all_to_all(first, "tensor", 0, 0, tiled=True)
    first = first.reshape(tensor_size, rank_dim, seg_len + key_shard)
    projected_own = jnp.sum(first[:, :, :seg_len], axis=0).astype(bf16)
    up_own = jnp.transpose(first[:, :, seg_len:], (1, 0, 2)).reshape(rank_dim, key_width)
    up_own = up_own.astype(bf16)

    own_live = position < live_segments[0]
    masked_own = jnp.where(own_live, output_grad, jnp.zeros_like(output_grad))
    lowrank_own = lax.dot_general(
        masked_own, up_own, (((1,), (1,)), ((), ())), preferred_element_type=f32
    ).astype(bf16)
    seg_up_own = 2.0 * jnp.dot(projected_own, masked_own, preferred_element_type=f32)

    low_spread = jnp.broadcast_to(
        lowrank_own.reshape(1, row_count * rank_dim), (tensor_size, row_count * rank_dim)
    )
    up_pieces = jnp.transpose(
        seg_up_own.reshape(rank_dim, tensor_size, key_shard), (1, 0, 2)
    ).reshape(tensor_size, rank_dim * key_shard)
    up_round = lax.reduce_precision(up_pieces, exponent_bits=8, mantissa_bits=7)
    up_high = up_round.astype(bf16)
    up_low = (up_pieces - up_round).astype(bf16)
    second = jnp.concatenate([low_spread, up_high, up_low], axis=1)
    second = second.reshape(tensor_size, -1, 128)
    second = lax.all_to_all(second, "tensor", 0, 0, tiled=True).reshape(tensor_size, -1)
    lowrank = second[:, : row_count * rank_dim].reshape(seg_group, seg_len, rank_dim)
    piece = rank_dim * key_shard
    low_end = row_count * rank_dim
    seg_up = second[:, low_end : low_end + piece].astype(f32)
    seg_up = seg_up + second[:, low_end + piece :].astype(f32)
    seg_up = seg_up.reshape(seg_group, rank_dim, key_shard)

    seg_down = 2.0 * jnp.einsum("sjr,sjd->srd", lowrank, input_seg, preferred_element_type=f32)
    seg_grad = jnp.concatenate([seg_down, seg_up], axis=2)
    onehot = (slot_ids[:, None] == seg_slot[None, :]).astype(bf16)
    grad_round = lax.reduce_precision(seg_grad, exponent_bits=8, mantissa_bits=7)
    grad_high = grad_round.astype(bf16)
    grad_low = (seg_grad - grad_round).astype(bf16)
    flat_high = grad_high.reshape(seg_group, -1)
    flat_low = grad_low.reshape(seg_group, -1)
    part = jnp.dot(onehot, flat_high, preferred_element_type=f32)
    part = part + jnp.dot(onehot, flat_low, preferred_element_type=f32)
    part = part.astype(bf16).reshape(group_count, per_owner, -1)
    gathered = lax.all_to_all(part, "dp", 0, 0, tiled=True)
    tok_live = jnp.repeat(seg_live, seg_len)[:, None]
    frozen = None
    for rows, weight in (
        (whole_first, key_weight[:, :half_key]),
        (whole_second, key_weight[:, half_key:]),
    ):
        rows = jnp.where(tok_live, rows, jnp.zeros_like(rows))
        step = lax.dot_general(
            rows, weight, (((1,), (1,)), ((), ())), preferred_element_type=f32
        )
        frozen = step if frozen is None else frozen + step
    extra = jnp.einsum("sjr,srd->sjd", lowrank, down_seg, preferred_element_type=f32)
    input_grad = (frozen + 2.0 * extra.reshape(tok_group, width_shard)).astype(bf16)
    gathered, input_grad = lax.optimization_barrier((gathered, input_grad))
    total = jnp.sum(gathered.astype(f32), axis=0).reshape(per_owner, rank_dim, -1)
    down_grad = total[:, :, :width_shard].astype(bf16)
    up_grad = total[:, :, width_shard:].astype(bf16)

    return (input_grad, down_grad, up_grad)


def solution(mesh):
    in_specs = (
        P("dp", "tensor"),
        P(("dp", "tensor"), None),
        P("tensor", None),
        P("dp", None, "tensor"),
        P("dp", None, "tensor"),
        P(),
        P(),
        P("dp"),
    )
    out_specs = (P("dp", "tensor"), P("dp", None, "tensor"), P("dp", None, "tensor"))
    return jax.shard_map(
        on_device, mesh=mesh, in_specs=in_specs, out_specs=out_specs, check_vma=False
    )
```

```python
import jax
import jax.numpy as jnp
from jax import lax
from jax.sharding import PartitionSpec as P


def on_device(
    layer_input,
    output_grad,
    key_weight,
    adapter_down,
    adapter_up,
    segment_adapter,
    adapter_slot,
    live_segments,
):
    tensor_size = lax.axis_size("tensor")
    position = lax.axis_index("tensor")
    group_count = lax.axis_size("dp")
    group_index = lax.axis_index("dp")
    row_count = output_grad.shape[0]
    tok_group = layer_input.shape[0]
    width_shard = layer_input.shape[1]
    key_width = output_grad.shape[1]
    key_shard = key_width // tensor_size
    adapters = adapter_slot.shape[0]
    rank_dim = adapter_down.shape[1]
    per_owner = adapter_down.shape[0]
    seg_total = segment_adapter.shape[0]
    seg_group = seg_total // group_count
    seg_len = tok_group // seg_group
    f32 = jnp.float32
    bf16 = jnp.bfloat16

    whole_raw = lax.all_gather(output_grad, "tensor", axis=0, tiled=True)

    slot_ids = jnp.arange(adapters, dtype=jnp.int32)
    lookup = segment_adapter[:, None] == slot_ids[None, :]
    every_slot = jnp.sum(jnp.where(lookup, adapter_slot[None, :], 0), axis=1)
    seg_slot = lax.dynamic_slice_in_dim(every_slot, group_index * seg_group, seg_group)
    seg_live = jnp.arange(seg_group, dtype=jnp.int32) < live_segments[0]

    local_store = jnp.concatenate([adapter_down, adapter_up], axis=2).reshape(per_owner, -1)
    spread = jnp.broadcast_to(local_store[None], (group_count,) + local_store.shape)
    stores = lax.all_to_all(spread, "dp", 0, 0, tiled=True).reshape(adapters, -1)
    choose = (seg_slot[:, None] == slot_ids[None, :]).astype(bf16)
    seg_store = jnp.dot(choose, stores, preferred_element_type=f32).astype(bf16)
    seg_store = seg_store.reshape(seg_group, rank_dim, width_shard + key_shard)
    down_seg = seg_store[:, :, :width_shard]
    up_seg = seg_store[:, :, width_shard:]

    input_seg = layer_input.reshape(seg_group, seg_len, width_shard)
    proj_part = jnp.einsum("sjd,srd->srj", input_seg, down_seg, preferred_element_type=f32)
    first = jnp.concatenate([proj_part, up_seg.astype(f32)], axis=2).reshape(seg_group, -1)
    first = lax.all_to_all(first, "tensor", 0, 0, tiled=True)
    first = first.reshape(tensor_size, rank_dim, seg_len + key_shard)
    projected_own = jnp.sum(first[:, :, :seg_len], axis=0).astype(bf16)
    up_own = jnp.transpose(first[:, :, seg_len:], (1, 0, 2)).reshape(rank_dim, key_width)
    up_own = up_own.astype(bf16)

    own_live = position < live_segments[0]
    masked_own = jnp.where(own_live, output_grad, jnp.zeros_like(output_grad))
    lowrank_own = lax.dot_general(
        masked_own, up_own, (((1,), (1,)), ((), ())), preferred_element_type=f32
    ).astype(bf16)
    seg_up_own = 2.0 * jnp.dot(projected_own, masked_own, preferred_element_type=f32)

    low_spread = jnp.broadcast_to(
        lowrank_own.reshape(1, row_count * rank_dim), (tensor_size, row_count * rank_dim)
    )
    up_pieces = jnp.transpose(
        seg_up_own.reshape(rank_dim, tensor_size, key_shard), (1, 0, 2)
    ).reshape(tensor_size, rank_dim * key_shard)
    up_round = lax.reduce_precision(up_pieces, exponent_bits=8, mantissa_bits=7)
    up_high = up_round.astype(bf16)
    up_low = (up_pieces - up_round).astype(bf16)
    second = jnp.concatenate([low_spread, up_high, up_low], axis=1)
    second = second.reshape(tensor_size, -1, 128)
    second = lax.all_to_all(second, "tensor", 0, 0, tiled=True).reshape(tensor_size, -1)
    lowrank = second[:, : row_count * rank_dim].reshape(seg_group, seg_len, rank_dim)
    piece = rank_dim * key_shard
    low_end = row_count * rank_dim
    seg_up = second[:, low_end : low_end + piece].astype(f32)
    seg_up = seg_up + second[:, low_end + piece :].astype(f32)
    seg_up = seg_up.reshape(seg_group, rank_dim, key_shard)

    seg_down = 2.0 * jnp.einsum("sjr,sjd->srd", lowrank, input_seg, preferred_element_type=f32)
    seg_grad = jnp.concatenate([seg_down, seg_up], axis=2)
    onehot = (slot_ids[:, None] == seg_slot[None, :]).astype(bf16)
    grad_round = lax.reduce_precision(seg_grad, exponent_bits=8, mantissa_bits=7)
    grad_high = grad_round.astype(bf16)
    grad_low = (seg_grad - grad_round).astype(bf16)
    flat_high = grad_high.reshape(seg_group, -1)
    flat_low = grad_low.reshape(seg_group, -1)
    part = jnp.dot(onehot, flat_high, preferred_element_type=f32)
    part = part + jnp.dot(onehot, flat_low, preferred_element_type=f32)
    part = part.astype(bf16).reshape(group_count, per_owner, -1)
    gathered = lax.all_to_all(part, "dp", 0, 0, tiled=True)
    frozen = lax.dot_general(
        whole_raw, key_weight, (((1,), (1,)), ((), ())), preferred_element_type=f32
    )
    frozen = jnp.where(jnp.repeat(seg_live, seg_len)[:, None], frozen, jnp.zeros_like(frozen))
    extra = jnp.einsum("sjr,srd->sjd", lowrank, down_seg, preferred_element_type=f32)
    input_grad = (frozen + 2.0 * extra.reshape(tok_group, width_shard)).astype(bf16)
    gathered, input_grad = lax.optimization_barrier((gathered, input_grad))
    total = jnp.sum(gathered.astype(f32), axis=0).reshape(per_owner, rank_dim, -1)
    down_grad = total[:, :, :width_shard].astype(bf16)
    up_grad = total[:, :, width_shard:].astype(bf16)

    return (input_grad, down_grad, up_grad)


def solution(mesh):
    in_specs = (
        P("dp", "tensor"),
        P(("dp", "tensor"), None),
        P("tensor", None),
        P("dp", None, "tensor"),
        P("dp", None, "tensor"),
        P(),
        P(),
        P("dp"),
    )
    out_specs = (P("dp", "tensor"), P("dp", None, "tensor"), P("dp", None, "tensor"))
    return jax.shard_map(
        on_device, mesh=mesh, in_specs=in_specs, out_specs=out_specs, check_vma=False
    )
```

```python
import jax
import jax.numpy as jnp
from jax import lax
from jax.sharding import PartitionSpec as P


def on_device(
    layer_input,
    output_grad,
    key_weight,
    adapter_down,
    adapter_up,
    segment_adapter,
    adapter_slot,
    live_segments,
):
    tensor_size = lax.axis_size("tensor")
    position = lax.axis_index("tensor")
    group_count = lax.axis_size("dp")
    group_index = lax.axis_index("dp")
    row_count = output_grad.shape[0]
    tok_group = layer_input.shape[0]
    width_shard = layer_input.shape[1]
    key_width = output_grad.shape[1]
    key_shard = key_width // tensor_size
    adapters = adapter_slot.shape[0]
    rank_dim = adapter_down.shape[1]
    per_owner = adapter_down.shape[0]
    seg_total = segment_adapter.shape[0]
    seg_group = seg_total // group_count
    seg_len = tok_group // seg_group
    f32 = jnp.float32
    bf16 = jnp.bfloat16

    whole_raw = lax.all_gather(output_grad, "tensor", axis=0, tiled=True)

    slot_ids = jnp.arange(adapters, dtype=jnp.int32)
    lookup = segment_adapter[:, None] == slot_ids[None, :]
    every_slot = jnp.sum(jnp.where(lookup, adapter_slot[None, :], 0), axis=1)
    seg_slot = lax.dynamic_slice_in_dim(every_slot, group_index * seg_group, seg_group)
    seg_live = jnp.arange(seg_group, dtype=jnp.int32) < live_segments[0]

    local_store = jnp.concatenate([adapter_down, adapter_up], axis=2).reshape(per_owner, -1)
    spread = jnp.broadcast_to(local_store[None], (group_count,) + local_store.shape)
    stores = lax.all_to_all(spread, "dp", 0, 0, tiled=True).reshape(adapters, -1)
    choose = (seg_slot[:, None] == slot_ids[None, :]).astype(bf16)
    seg_store = jnp.dot(choose, stores, preferred_element_type=f32).astype(bf16)
    seg_store = seg_store.reshape(seg_group, rank_dim, width_shard + key_shard)
    down_seg = seg_store[:, :, :width_shard]
    up_seg = seg_store[:, :, width_shard:]

    input_seg = layer_input.reshape(seg_group, seg_len, width_shard)
    proj_part = jnp.einsum("sjd,srd->srj", input_seg, down_seg, preferred_element_type=f32)
    first = jnp.concatenate([proj_part, up_seg.astype(f32)], axis=2).reshape(seg_group, -1)
    first = lax.all_to_all(first, "tensor", 0, 0, tiled=True)
    first = first.reshape(tensor_size, rank_dim, seg_len + key_shard)
    projected_own = jnp.sum(first[:, :, :seg_len], axis=0).astype(bf16)
    up_own = jnp.transpose(first[:, :, seg_len:], (1, 0, 2)).reshape(rank_dim, key_width)
    up_own = up_own.astype(bf16)

    own_live = position < live_segments[0]
    masked_own = jnp.where(own_live, output_grad, jnp.zeros_like(output_grad))
    lowrank_own = lax.dot_general(
        masked_own, up_own, (((1,), (1,)), ((), ())), preferred_element_type=f32
    ).astype(bf16)
    seg_up_own = 2.0 * jnp.dot(projected_own, masked_own, preferred_element_type=f32)

    low_spread = jnp.broadcast_to(
        lowrank_own.reshape(1, row_count * rank_dim), (tensor_size, row_count * rank_dim)
    )
    up_pieces = jnp.transpose(
        seg_up_own.reshape(rank_dim, tensor_size, key_shard), (1, 0, 2)
    ).reshape(tensor_size, rank_dim * key_shard)
    up_round = lax.reduce_precision(up_pieces, exponent_bits=8, mantissa_bits=7)
    up_high = up_round.astype(bf16)
    up_low = (up_pieces - up_round).astype(bf16)
    second = jnp.concatenate([low_spread, up_high, up_low], axis=1)
    second = second.reshape(tensor_size, 1, -1)
    second = lax.all_to_all(second, "tensor", 0, 0, tiled=True).reshape(tensor_size, -1)
    lowrank = second[:, : row_count * rank_dim].reshape(seg_group, seg_len, rank_dim)
    piece = rank_dim * key_shard
    low_end = row_count * rank_dim
    seg_up = second[:, low_end : low_end + piece].astype(f32)
    seg_up = seg_up + second[:, low_end + piece :].astype(f32)
    seg_up = seg_up.reshape(seg_group, rank_dim, key_shard)

    seg_down = 2.0 * jnp.einsum("sjr,sjd->srd", lowrank, input_seg, preferred_element_type=f32)
    seg_grad = jnp.concatenate([seg_down, seg_up], axis=2)
    onehot = (slot_ids[:, None] == seg_slot[None, :]).astype(bf16)
    grad_round = lax.reduce_precision(seg_grad, exponent_bits=8, mantissa_bits=7)
    grad_high = grad_round.astype(bf16)
    grad_low = (seg_grad - grad_round).astype(bf16)
    flat_high = grad_high.reshape(seg_group, -1)
    flat_low = grad_low.reshape(seg_group, -1)
    part = jnp.dot(onehot, flat_high, preferred_element_type=f32)
    part = part + jnp.dot(onehot, flat_low, preferred_element_type=f32)
    part = part.astype(bf16).reshape(group_count, per_owner, -1)
    gathered = lax.all_to_all(part, "dp", 0, 0, tiled=True)
    frozen = lax.dot_general(
        whole_raw, key_weight, (((1,), (1,)), ((), ())), preferred_element_type=f32
    )
    frozen = jnp.where(jnp.repeat(seg_live, seg_len)[:, None], frozen, jnp.zeros_like(frozen))
    extra = jnp.einsum("sjr,srd->sjd", lowrank, down_seg, preferred_element_type=f32)
    input_grad = (frozen + 2.0 * extra.reshape(tok_group, width_shard)).astype(bf16)
    gathered, input_grad = lax.optimization_barrier((gathered, input_grad))
    total = jnp.sum(gathered.astype(f32), axis=0).reshape(per_owner, rank_dim, -1)
    down_grad = total[:, :, :width_shard].astype(bf16)
    up_grad = total[:, :, width_shard:].astype(bf16)

    return (input_grad, down_grad, up_grad)


def solution(mesh):
    in_specs = (
        P("dp", "tensor"),
        P(("dp", "tensor"), None),
        P("tensor", None),
        P("dp", None, "tensor"),
        P("dp", None, "tensor"),
        P(),
        P(),
        P("dp"),
    )
    out_specs = (P("dp", "tensor"), P("dp", None, "tensor"), P("dp", None, "tensor"))
    return jax.shard_map(
        on_device, mesh=mesh, in_specs=in_specs, out_specs=out_specs, check_vma=False
    )
```

```python
import jax
import jax.numpy as jnp
from jax import lax
from jax.sharding import PartitionSpec as P


def on_device(
    layer_input,
    output_grad,
    key_weight,
    adapter_down,
    adapter_up,
    segment_adapter,
    adapter_slot,
    live_segments,
):
    tensor_size = lax.axis_size("tensor")
    position = lax.axis_index("tensor")
    group_count = lax.axis_size("dp")
    group_index = lax.axis_index("dp")
    row_count = output_grad.shape[0]
    tok_group = layer_input.shape[0]
    width_shard = layer_input.shape[1]
    key_width = output_grad.shape[1]
    key_shard = key_width // tensor_size
    adapters = adapter_slot.shape[0]
    rank_dim = adapter_down.shape[1]
    per_owner = adapter_down.shape[0]
    seg_total = segment_adapter.shape[0]
    seg_group = seg_total // group_count
    seg_len = tok_group // seg_group
    f32 = jnp.float32
    bf16 = jnp.bfloat16

    whole_raw = lax.all_gather(output_grad, "tensor", axis=0, tiled=True)

    slot_ids = jnp.arange(adapters, dtype=jnp.int32)
    lookup = segment_adapter[:, None] == slot_ids[None, :]
    every_slot = jnp.sum(jnp.where(lookup, adapter_slot[None, :], 0), axis=1)
    seg_slot = lax.dynamic_slice_in_dim(every_slot, group_index * seg_group, seg_group)
    seg_live = jnp.arange(seg_group, dtype=jnp.int32) < live_segments[0]

    local_store = jnp.concatenate([adapter_down, adapter_up], axis=2).reshape(per_owner, -1)
    spread = jnp.broadcast_to(local_store[None], (group_count,) + local_store.shape)
    stores = lax.all_to_all(spread, "dp", 0, 0, tiled=True).reshape(adapters, -1)
    choose = (seg_slot[:, None] == slot_ids[None, :]).astype(bf16)
    seg_store = jnp.dot(choose, stores, preferred_element_type=f32).astype(bf16)
    seg_store = seg_store.reshape(seg_group, rank_dim, width_shard + key_shard)
    down_seg = seg_store[:, :, :width_shard]
    up_seg = seg_store[:, :, width_shard:]

    input_seg = layer_input.reshape(seg_group, seg_len, width_shard)
    proj_part = jnp.einsum("sjd,srd->srj", input_seg, down_seg, preferred_element_type=f32)
    first = jnp.concatenate([proj_part.astype(bf16), up_seg], axis=2).reshape(seg_group, -1)
    first = lax.all_to_all(first, "tensor", 0, 0, tiled=True)
    first = first.reshape(tensor_size, rank_dim, seg_len + key_shard)
    projected_own = jnp.sum(first[:, :, :seg_len].astype(f32), axis=0).astype(bf16)
    up_own = jnp.transpose(first[:, :, seg_len:], (1, 0, 2)).reshape(rank_dim, key_width)

    own_live = position < live_segments[0]
    masked_own = jnp.where(own_live, output_grad, jnp.zeros_like(output_grad))
    lowrank_own = lax.dot_general(
        masked_own, up_own, (((1,), (1,)), ((), ())), preferred_element_type=f32
    ).astype(bf16)
    seg_up_own = 2.0 * jnp.dot(projected_own, masked_own, preferred_element_type=f32)

    low_spread = jnp.broadcast_to(
        lowrank_own.reshape(1, row_count * rank_dim), (tensor_size, row_count * rank_dim)
    )
    up_pieces = jnp.transpose(
        seg_up_own.reshape(rank_dim, tensor_size, key_shard), (1, 0, 2)
    ).reshape(tensor_size, rank_dim * key_shard)
    up_round = lax.reduce_precision(up_pieces, exponent_bits=8, mantissa_bits=7)
    up_high = up_round.astype(bf16)
    up_low = (up_pieces - up_round).astype(bf16)
    second = jnp.concatenate([low_spread, up_high, up_low], axis=1)
    second = second.reshape(tensor_size, -1, 128)
    second = lax.all_to_all(second, "tensor", 0, 0, tiled=True).reshape(tensor_size, -1)
    lowrank = second[:, : row_count * rank_dim].reshape(seg_group, seg_len, rank_dim)
    piece = rank_dim * key_shard
    low_end = row_count * rank_dim
    seg_up = second[:, low_end : low_end + piece].astype(f32)
    seg_up = seg_up + second[:, low_end + piece :].astype(f32)
    seg_up = seg_up.reshape(seg_group, rank_dim, key_shard)

    seg_down = 2.0 * jnp.einsum("sjr,sjd->srd", lowrank, input_seg, preferred_element_type=f32)
    seg_grad = jnp.concatenate([seg_down, seg_up], axis=2)
    onehot = (slot_ids[:, None] == seg_slot[None, :]).astype(bf16)
    grad_round = lax.reduce_precision(seg_grad, exponent_bits=8, mantissa_bits=7)
    grad_high = grad_round.astype(bf16)
    grad_low = (seg_grad - grad_round).astype(bf16)
    flat_high = grad_high.reshape(seg_group, -1)
    flat_low = grad_low.reshape(seg_group, -1)
    part = jnp.dot(onehot, flat_high, preferred_element_type=f32)
    part = part + jnp.dot(onehot, flat_low, preferred_element_type=f32)
    part = part.astype(bf16).reshape(group_count, per_owner, -1)
    gathered = lax.all_to_all(part, "dp", 0, 0, tiled=True)
    frozen = lax.dot_general(
        whole_raw, key_weight, (((1,), (1,)), ((), ())), preferred_element_type=f32
    )
    frozen = jnp.where(jnp.repeat(seg_live, seg_len)[:, None], frozen, jnp.zeros_like(frozen))
    extra = jnp.einsum("sjr,srd->sjd", lowrank, down_seg, preferred_element_type=f32)
    input_grad = (frozen + 2.0 * extra.reshape(tok_group, width_shard)).astype(bf16)
    gathered, input_grad = lax.optimization_barrier((gathered, input_grad))
    total = jnp.sum(gathered.astype(f32), axis=0).reshape(per_owner, rank_dim, -1)
    down_grad = total[:, :, :width_shard].astype(bf16)
    up_grad = total[:, :, width_shard:].astype(bf16)

    return (input_grad, down_grad, up_grad)


def solution(mesh):
    in_specs = (
        P("dp", "tensor"),
        P(("dp", "tensor"), None),
        P("tensor", None),
        P("dp", None, "tensor"),
        P("dp", None, "tensor"),
        P(),
        P(),
        P("dp"),
    )
    out_specs = (P("dp", "tensor"), P("dp", None, "tensor"), P("dp", None, "tensor"))
    return jax.shard_map(
        on_device, mesh=mesh, in_specs=in_specs, out_specs=out_specs, check_vma=False
    )
```

```python
import jax
import jax.numpy as jnp
from jax import lax
from jax.sharding import PartitionSpec as P


def on_device(
    layer_input,
    output_grad,
    key_weight,
    adapter_down,
    adapter_up,
    segment_adapter,
    adapter_slot,
    live_segments,
):
    tensor_size = lax.axis_size("tensor")
    position = lax.axis_index("tensor")
    group_count = lax.axis_size("dp")
    group_index = lax.axis_index("dp")
    row_count = output_grad.shape[0]
    tok_group = layer_input.shape[0]
    width_shard = layer_input.shape[1]
    key_width = output_grad.shape[1]
    key_shard = key_width // tensor_size
    adapters = adapter_slot.shape[0]
    rank_dim = adapter_down.shape[1]
    per_owner = adapter_down.shape[0]
    seg_total = segment_adapter.shape[0]
    seg_group = seg_total // group_count
    seg_len = tok_group // seg_group
    f32 = jnp.float32
    bf16 = jnp.bfloat16

    whole_raw = lax.all_gather(output_grad, "tensor", axis=0, tiled=True)

    slot_ids = jnp.arange(adapters, dtype=jnp.int32)
    lookup = segment_adapter[:, None] == slot_ids[None, :]
    every_slot = jnp.sum(jnp.where(lookup, adapter_slot[None, :], 0), axis=1)
    seg_slot = lax.dynamic_slice_in_dim(every_slot, group_index * seg_group, seg_group)
    seg_live = jnp.arange(seg_group, dtype=jnp.int32) < live_segments[0]

    local_store = jnp.concatenate([adapter_down, adapter_up], axis=2).reshape(per_owner, -1)
    spread = jnp.broadcast_to(local_store[None], (group_count,) + local_store.shape)
    stores = lax.all_to_all(spread, "dp", 0, 0, tiled=True).reshape(adapters, -1)
    choose = (seg_slot[:, None] == slot_ids[None, :]).astype(bf16)
    seg_store = jnp.dot(choose, stores, preferred_element_type=f32).astype(bf16)
    seg_store = seg_store.reshape(seg_group, rank_dim, width_shard + key_shard)
    down_seg = seg_store[:, :, :width_shard]
    up_seg = seg_store[:, :, width_shard:]

    input_seg = layer_input.reshape(seg_group, seg_len, width_shard)
    proj_part = jnp.einsum("sjd,srd->srj", input_seg, down_seg, preferred_element_type=f32)
    first = jnp.concatenate([proj_part, up_seg.astype(f32)], axis=2).reshape(seg_group, -1, 128)
    first = lax.all_to_all(first, "tensor", 0, 0, tiled=True)
    first = first.reshape(tensor_size, rank_dim, seg_len + key_shard)
    projected_own = jnp.sum(first[:, :, :seg_len], axis=0).astype(bf16)
    up_own = jnp.transpose(first[:, :, seg_len:], (1, 0, 2)).reshape(rank_dim, key_width)
    up_own = up_own.astype(bf16)

    own_live = position < live_segments[0]
    masked_own = jnp.where(own_live, output_grad, jnp.zeros_like(output_grad))
    lowrank_own = lax.dot_general(
        masked_own, up_own, (((1,), (1,)), ((), ())), preferred_element_type=f32
    ).astype(bf16)
    seg_up_own = 2.0 * jnp.dot(projected_own, masked_own, preferred_element_type=f32)

    low_spread = jnp.broadcast_to(
        lowrank_own.reshape(1, row_count * rank_dim), (tensor_size, row_count * rank_dim)
    )
    up_pieces = jnp.transpose(
        seg_up_own.reshape(rank_dim, tensor_size, key_shard), (1, 0, 2)
    ).reshape(tensor_size, rank_dim * key_shard)
    up_round = lax.reduce_precision(up_pieces, exponent_bits=8, mantissa_bits=7)
    up_high = up_round.astype(bf16)
    up_low = (up_pieces - up_round).astype(bf16)
    second = jnp.concatenate([low_spread, up_high, up_low], axis=1)
    second = second.reshape(tensor_size, -1, 128)
    second = lax.all_to_all(second, "tensor", 0, 0, tiled=True).reshape(tensor_size, -1)
    lowrank = second[:, : row_count * rank_dim].reshape(seg_group, seg_len, rank_dim)
    piece = rank_dim * key_shard
    low_end = row_count * rank_dim
    seg_up = second[:, low_end : low_end + piece].astype(f32)
    seg_up = seg_up + second[:, low_end + piece :].astype(f32)
    seg_up = seg_up.reshape(seg_group, rank_dim, key_shard)

    seg_down = 2.0 * jnp.einsum("sjr,sjd->srd", lowrank, input_seg, preferred_element_type=f32)
    seg_grad = jnp.concatenate([seg_down, seg_up], axis=2)
    onehot = (slot_ids[:, None] == seg_slot[None, :]).astype(bf16)
    grad_round = lax.reduce_precision(seg_grad, exponent_bits=8, mantissa_bits=7)
    grad_high = grad_round.astype(bf16)
    grad_low = (seg_grad - grad_round).astype(bf16)
    flat_high = grad_high.reshape(seg_group, -1)
    flat_low = grad_low.reshape(seg_group, -1)
    part = jnp.dot(onehot, flat_high, preferred_element_type=f32)
    part = part + jnp.dot(onehot, flat_low, preferred_element_type=f32)
    part = part.astype(bf16).reshape(group_count, per_owner, -1)
    gathered = lax.all_to_all(part, "dp", 0, 0, tiled=True)
    frozen = lax.dot_general(
        whole_raw, key_weight, (((1,), (1,)), ((), ())), preferred_element_type=f32
    )
    frozen = jnp.where(jnp.repeat(seg_live, seg_len)[:, None], frozen, jnp.zeros_like(frozen))
    extra = jnp.einsum("sjr,srd->sjd", lowrank, down_seg, preferred_element_type=f32)
    input_grad = (frozen + 2.0 * extra.reshape(tok_group, width_shard)).astype(bf16)
    gathered, input_grad = lax.optimization_barrier((gathered, input_grad))
    total = jnp.sum(gathered.astype(f32), axis=0).reshape(per_owner, rank_dim, -1)
    down_grad = total[:, :, :width_shard].astype(bf16)
    up_grad = total[:, :, width_shard:].astype(bf16)

    return (input_grad, down_grad, up_grad)


def solution(mesh):
    in_specs = (
        P("dp", "tensor"),
        P(("dp", "tensor"), None),
        P("tensor", None),
        P("dp", None, "tensor"),
        P("dp", None, "tensor"),
        P(),
        P(),
        P("dp"),
    )
    out_specs = (P("dp", "tensor"), P("dp", None, "tensor"), P("dp", None, "tensor"))
    return jax.shard_map(
        on_device, mesh=mesh, in_specs=in_specs, out_specs=out_specs, check_vma=False
    )
```

```python
import jax
import jax.numpy as jnp
from jax import lax
from jax.sharding import PartitionSpec as P


def on_device(
    layer_input,
    output_grad,
    key_weight,
    adapter_down,
    adapter_up,
    segment_adapter,
    adapter_slot,
    live_segments,
):
    tensor_size = lax.axis_size("tensor")
    position = lax.axis_index("tensor")
    group_count = lax.axis_size("dp")
    group_index = lax.axis_index("dp")
    row_count = output_grad.shape[0]
    tok_group = layer_input.shape[0]
    width_shard = layer_input.shape[1]
    key_width = output_grad.shape[1]
    key_shard = key_width // tensor_size
    adapters = adapter_slot.shape[0]
    rank_dim = adapter_down.shape[1]
    per_owner = adapter_down.shape[0]
    seg_total = segment_adapter.shape[0]
    seg_group = seg_total // group_count
    seg_len = tok_group // seg_group
    f32 = jnp.float32
    bf16 = jnp.bfloat16

    whole_raw = lax.all_gather(output_grad, "tensor", axis=0, tiled=True)

    slot_ids = jnp.arange(adapters, dtype=jnp.int32)
    lookup = segment_adapter[:, None] == slot_ids[None, :]
    every_slot = jnp.sum(jnp.where(lookup, adapter_slot[None, :], 0), axis=1)
    seg_slot = lax.dynamic_slice_in_dim(every_slot, group_index * seg_group, seg_group)
    seg_live = jnp.arange(seg_group, dtype=jnp.int32) < live_segments[0]

    local_store = jnp.concatenate([adapter_down, adapter_up], axis=2).reshape(per_owner, -1)
    spread = jnp.broadcast_to(local_store[None], (group_count,) + local_store.shape)
    stores = lax.all_to_all(spread, "dp", 0, 0, tiled=True).reshape(adapters, -1)
    choose = (seg_slot[:, None] == slot_ids[None, :]).astype(bf16)
    seg_store = jnp.dot(choose, stores, preferred_element_type=f32).astype(bf16)
    seg_store = seg_store.reshape(seg_group, rank_dim, width_shard + key_shard)
    down_seg = seg_store[:, :, :width_shard]
    up_seg = seg_store[:, :, width_shard:]

    input_seg = layer_input.reshape(seg_group, seg_len, width_shard)
    proj_part = jnp.einsum("sjd,srd->srj", input_seg, down_seg, preferred_element_type=f32)
    first = jnp.concatenate([proj_part, up_seg.astype(f32)], axis=2).reshape(seg_group, -1)
    first = lax.all_to_all(first, "tensor", 0, 0, tiled=True)
    first = first.reshape(tensor_size, rank_dim, seg_len + key_shard)
    projected_own = jnp.sum(first[:, :, :seg_len], axis=0).astype(bf16)
    up_own = jnp.transpose(first[:, :, seg_len:], (1, 0, 2)).reshape(rank_dim, key_width)
    up_own = up_own.astype(bf16)

    own_live = position < live_segments[0]
    masked_own = jnp.where(own_live, output_grad, jnp.zeros_like(output_grad))
    lowrank_own = lax.dot_general(
        up_own, masked_own, (((1,), (1,)), ((), ())), preferred_element_type=f32
    ).astype(bf16)
    seg_up_own = 2.0 * jnp.dot(projected_own, masked_own, preferred_element_type=f32)

    low_spread = jnp.broadcast_to(
        lowrank_own.reshape(1, row_count * rank_dim), (tensor_size, row_count * rank_dim)
    )
    up_pieces = jnp.transpose(
        seg_up_own.reshape(rank_dim, tensor_size, key_shard), (1, 0, 2)
    ).reshape(tensor_size, rank_dim * key_shard)
    up_round = lax.reduce_precision(up_pieces, exponent_bits=8, mantissa_bits=7)
    up_high = up_round.astype(bf16)
    up_low = (up_pieces - up_round).astype(bf16)
    second = jnp.concatenate([low_spread, up_high, up_low], axis=1)
    second = second.reshape(tensor_size, -1, 128)
    second = lax.all_to_all(second, "tensor", 0, 0, tiled=True).reshape(tensor_size, -1)
    lowrank = second[:, : row_count * rank_dim].reshape(seg_group, rank_dim, seg_len)
    piece = rank_dim * key_shard
    low_end = row_count * rank_dim
    seg_up = second[:, low_end : low_end + piece].astype(f32)
    seg_up = seg_up + second[:, low_end + piece :].astype(f32)
    seg_up = seg_up.reshape(seg_group, rank_dim, key_shard)

    seg_down = 2.0 * jnp.einsum("srj,sjd->srd", lowrank, input_seg, preferred_element_type=f32)
    seg_grad = jnp.concatenate([seg_down, seg_up], axis=2)
    onehot = (slot_ids[:, None] == seg_slot[None, :]).astype(bf16)
    grad_round = lax.reduce_precision(seg_grad, exponent_bits=8, mantissa_bits=7)
    grad_high = grad_round.astype(bf16)
    grad_low = (seg_grad - grad_round).astype(bf16)
    flat_high = grad_high.reshape(seg_group, -1)
    flat_low = grad_low.reshape(seg_group, -1)
    part = jnp.dot(onehot, flat_high, preferred_element_type=f32)
    part = part + jnp.dot(onehot, flat_low, preferred_element_type=f32)
    part = part.astype(bf16).reshape(group_count, per_owner, -1)
    gathered = lax.all_to_all(part, "dp", 0, 0, tiled=True)
    frozen = lax.dot_general(
        whole_raw, key_weight, (((1,), (1,)), ((), ())), preferred_element_type=f32
    )
    frozen = jnp.where(jnp.repeat(seg_live, seg_len)[:, None], frozen, jnp.zeros_like(frozen))
    extra = jnp.einsum("srj,srd->sjd", lowrank, down_seg, preferred_element_type=f32)
    input_grad = (frozen + 2.0 * extra.reshape(tok_group, width_shard)).astype(bf16)
    gathered, input_grad = lax.optimization_barrier((gathered, input_grad))
    total = jnp.sum(gathered.astype(f32), axis=0).reshape(per_owner, rank_dim, -1)
    down_grad = total[:, :, :width_shard].astype(bf16)
    up_grad = total[:, :, width_shard:].astype(bf16)

    return (input_grad, down_grad, up_grad)


def solution(mesh):
    in_specs = (
        P("dp", "tensor"),
        P(("dp", "tensor"), None),
        P("tensor", None),
        P("dp", None, "tensor"),
        P("dp", None, "tensor"),
        P(),
        P(),
        P("dp"),
    )
    out_specs = (P("dp", "tensor"), P("dp", None, "tensor"), P("dp", None, "tensor"))
    return jax.shard_map(
        on_device, mesh=mesh, in_specs=in_specs, out_specs=out_specs, check_vma=False
    )
```
